32 devices in a mesh: sec: 4 (over y, x), dev: 8 (over z, core).
Axes of the slice: x: 2, y: 2, z: 4, core: 2. Of those that a mesh axis runs over, the one named last changes fastest.
Arguments:
- strain_rows: bfloat16 [65536, 128], P(('sec', 'dev')), may hold values from -6 to 6
- bands: int32 [65536], P(('sec', 'dev')), may hold values from 0 to 15
- damaged: int32 [4096], P(('sec', 'dev')), may hold values from 0 to 2047
- owner: int32 [4096, 1], P(('sec', 'dev')), may hold values from 0 to 31; in each aligned block of 128 rows (0 to 127, 128 to 255, ...) at most 8 rows name the same one
- first_layers: bfloat16 [4096, 4096], P(('sec', 'dev')), may hold values from -0.5 to 0.5
- middle_weight: bfloat16 [4096, 4096], P(None, 'sec'), may hold values from -0.09375 to 0.09375
- out_weight: bfloat16 [4096, 128], P('sec'), may hold values from -0.09375 to 0.09375
- band_scale: float32 [16, 4096], replicated, may hold values from 0.5 to 2
- back_weight: bfloat16 [128, 128], replicated, may hold values from -0.5 to 0.5
Outputs:
- response: bfloat16 [4096, 128], P(('sec', 'dev'))
The draws below stay inside these ranges and needn't reach their ends.
Inputs may be any that keep to these rules, and one draw needn't show every extreme that they name: Among the 128 rows of one macro device no owner is named more than 8 times, a bound that some block reaches. `damaged`: indices into the listing device's own 2048 points.
All inputs are finite; a program needn't handle non-finite values.
Results may differ from the reference program's by a relative error of at most 0.014.
Values may be sent and summed in bfloat16 or wider, within the bound.
No kernel may reach another device: no remote copies, remote signals or barrier semaphores. Data moves between devices by JAX's collectives and lax.ppermute only.
A program may use at most 128 MiB of HBM per device.

```python
import math
import jax
import jax.numpy as jnp
import numpy as np
from jax import lax

FEAT = 128
HID = 4096
OUT = 128
BANDS = 16
P_DEV = 2048
LIST_DEV = 128
PASSES = 2
POINTS = 65536
LISTED = 4096
CAP = 8
RECV = 256
DEVICES = 32


def touch_ends(entries, own_key, least, top_value):
    shape = entries.shape
    index_at = [jax.random.randint(jax.random.fold_in(own_key, axis), (), 0, shape[axis]) for axis in range(len(shape))]
    entries = entries.at[tuple(index_at)].set(least)
    longest = shape.index(max(shape))
    index_at[longest] = (index_at[longest] + 1) % shape[longest]
    return entries.at[tuple(index_at)].set(top_value)


def level_of(own_key, extent, cuts, smallest, largest):
    factor_of, own = 1.0, jax.random.fold_in(own_key, 6)
    for dim, parts in cuts:
        draws = jnp.exp(jax.random.uniform(jax.random.fold_in(own, dim), (parts,), jnp.float32, smallest / len(cuts), largest / len(cuts)))
        factor_of = factor_of * jnp.repeat(draws, extent[dim] // parts).reshape([-1 if axis == dim else 1 for axis in range(len(extent))])
    return factor_of


def shared_out(key, own, number, rows, number_of, top, reach, skew):
    sequence = jax.random.permutation(key, number_of)
    crowded, ordinary = load_shares(number_of, rows * top, reach, skew, True), load_shares(number_of, rows * top, reach, skew, False)
    places = jnp.arange(number_of)

    def named(tallies, rotation):
        used = int((tallies > 0).sum())
        fixed = max(1, used // 4)
        passed = fixed + (places - fixed + rotation * (used - fixed)) % max(1, number_of - fixed)
        return jnp.zeros((number_of,), jnp.int32).at[sequence[jnp.where(places < fixed, places, passed)]].set(jnp.asarray(tallies, jnp.int32))

    tallies = jnp.where(number % 4 == 0, named(crowded, number // 4), named(ordinary, number - number // 4 - 1))
    mixed = jax.random.permutation(jax.random.fold_in(own, 3), number_of)
    donor, taker = mixed[0:number_of // 2 * 2:2], mixed[1:number_of // 2 * 2:2]
    slack = jnp.minimum(tallies[donor] - 1, reach - tallies[taker]) // 2
    slack = jnp.where((donor == sequence[0]) | (taker == sequence[0]) | (tallies[taker] == 0), 0, jnp.maximum(slack, 0))
    passed = jax.random.randint(jax.random.fold_in(own, 4), (number_of // 2,), 0, 1 << 20) % (slack + 1)
    tallies = tallies.at[donor].add(-passed).at[taker].add(passed)
    labels = jnp.searchsorted(jnp.cumsum(tallies), jnp.arange(rows * top), side="right").astype(jnp.int32)
    listing = labels.reshape(top, rows).T
    listing = listing[jax.random.permutation(jax.random.fold_in(own, 1), rows)]
    rotation = jax.random.randint(jax.random.fold_in(own, 2), (rows, 1), 0, top)
    return jnp.take_along_axis(listing, (jnp.arange(top)[None, :] + rotation) % top, axis=1)


def load_shares(number_of, total, most, skew, full):
    weights = [(1 << 20) // math.isqrt(standing ** skew) + 1 for standing in range(1, number_of + 1)]
    largest = most if full else min(most, max(-(-total // number_of), total * weights[0] // sum(weights)))
    least = 1 if total - largest >= number_of - 1 else 0
    given, surplus = [largest] + [least] * (number_of - 1), total - largest - least * (number_of - 1)
    while surplus > 0:
        free = [i for i in range(1, number_of) if given[i] < largest] or [i for i in range(1, number_of) if given[i] < most]
        pool, budget = sum([weights[i] for i in free]), surplus
        for i in free:
            more = min(most - given[i], max(1, budget * weights[i] // pool), surplus)
            given[i] = given[i] + more
            surplus = surplus - more
    return np.array(given)


def noise(key, dims, deviation, reach, pieces=(), kind=jnp.bfloat16):
    values = jax.random.normal(key, dims, jnp.float32) * deviation
    if len(pieces) > 0:
        values = level_of(key, dims, pieces, -0.22, 0.18) * values
    return jnp.clip(values, min=-reach, max=reach).astype(kind)


def setup_inputs(seed: int = 0) -> dict:
    streams_of = jax.random.split(jax.random.key(seed), 10)
    strain_rows = noise(streams_of[0], (POINTS, FEAT), 1.0, 6.0, ((0, 32),))
    bands = touch_ends(jax.random.randint(streams_of[1], (POINTS,), 0, BANDS), jax.random.fold_in(streams_of[1], 1), 0, BANDS - 1).astype(jnp.int32)
    damaged = touch_ends(jax.random.randint(streams_of[2], (LISTED,), 0, P_DEV), jax.random.fold_in(streams_of[2], 1), 0, P_DEV - 1).astype(jnp.int32)
    owner_keys = jax.random.split(jax.random.fold_in(streams_of[3], 1), LISTED // LIST_DEV)
    owner_turns = jax.random.permutation(jax.random.fold_in(streams_of[3], 3), LISTED // LIST_DEV)
    owner = jax.vmap(lambda own, number: shared_out(jax.random.fold_in(streams_of[3], 2), own, number, LIST_DEV, DEVICES, 1, CAP, 2))(owner_keys, owner_turns).reshape((LISTED, 1))
    first_layers = noise(streams_of[4], (DEVICES * FEAT, HID), FEAT ** -0.5, 0.5, ((0, 32),))
    middle_weight = noise(streams_of[5], (HID, HID), HID ** -0.5, 0.09375, ((1, 4),))
    out_weight = noise(streams_of[6], (HID, OUT), HID ** -0.5, 0.09375, ((0, 4),))
    band_scale = jnp.clip(jnp.exp(jax.random.uniform(streams_of[7], (BANDS, HID), jnp.float32, math.log(0.5), math.log(2.0))), 0.5, 2.0)
    back_weight = noise(streams_of[8], (OUT, FEAT), OUT ** -0.5, 0.5)
    return dict(strain_rows=strain_rows, bands=bands, damaged=damaged, owner=owner, first_layers=first_layers, middle_weight=middle_weight, out_weight=out_weight, band_scale=band_scale, back_weight=back_weight)


def reference(strain_rows, bands, damaged, owner, first_layers, middle_weight, out_weight, band_scale, back_weight):
    listed = damaged.shape[0]
    point_index = (jnp.arange(listed, dtype=jnp.int32) // LIST_DEV) * P_DEV + damaged.astype(jnp.int32)
    features = strain_rows[point_index]
    point_band = bands[point_index]
    owners = owner[:, 0].astype(jnp.int32)
    ordering = jnp.argsort(owners, stable=True).astype(jnp.int32)
    counts = jnp.sum((owners[None, :] == jnp.arange(DEVICES, dtype=jnp.int32)[:, None]).astype(jnp.int32), axis=1)
    starts = jnp.cumsum(counts) - counts
    slot_index = jnp.arange(RECV, dtype=jnp.int32)
    position = jnp.minimum(starts[:, None] + slot_index[None, :], listed - 1).astype(jnp.int32)
    live_slot = slot_index[None, :] < counts[:, None]
    row_index = ordering[position]
    owner_weights = first_layers.reshape(DEVICES, FEAT, HID)
    target_rows = jnp.where(live_slot, row_index, listed).reshape(-1)
    result = None
    for segment_index in range(PASSES):
        def first_part(packed):
            weight_block, row_ids = packed
            block_rows = features[row_ids]
            scale_rows = band_scale[point_band[row_ids]]
            mixed = jnp.dot(block_rows, weight_block, preferred_element_type=jnp.float32) * scale_rows
            return jax.nn.silu(mixed).astype(jnp.bfloat16)

        per_owner = lax.map(first_part, (owner_weights, row_index))
        hidden = jnp.zeros((listed, HID), per_owner.dtype).at[target_rows].set(per_owner.reshape(-1, HID), mode="drop")

        def rest_part(hidden_block):
            middle = jax.nn.silu(jnp.dot(hidden_block, middle_weight, preferred_element_type=jnp.float32)).astype(jnp.bfloat16)
            return jnp.dot(middle, out_weight, preferred_element_type=jnp.float32).astype(jnp.bfloat16)

        result = lax.map(rest_part, hidden.reshape(listed // LIST_DEV, LIST_DEV, HID)).reshape(listed, OUT)
        features = (features.astype(jnp.float32) + jnp.dot(result, back_weight, preferred_element_type=jnp.float32)).astype(jnp.bfloat16)
    return result
```

```python
import jax
import jax.numpy as jnp
from jax import lax
from jax.sharding import PartitionSpec as P

PASSES = 2


def scale_parts(band_scale):
    hi = band_scale.astype(jnp.bfloat16)
    rest = band_scale - hi.astype(jnp.float32)
    mid = rest.astype(jnp.bfloat16)
    lo = (rest - mid.astype(jnp.float32)).astype(jnp.bfloat16)
    return jnp.concatenate([hi, mid, lo], axis=0)


def band_rows(band_values, parts):
    levels = parts.shape[0] // 3
    level_ids = jnp.arange(3 * levels, dtype=jnp.int32) % levels
    picks = (band_values[:, None] == level_ids[None, :]).astype(jnp.bfloat16)
    return jnp.dot(picks, parts, preferred_element_type=jnp.float32)


def first_hidden(rows, weights, band_values, parts):
    mixed = jnp.einsum("srf,sfh->srh", rows, weights, preferred_element_type=jnp.float32)
    mixed = mixed.reshape(-1, weights.shape[2]) * band_rows(band_values, parts)
    return jax.nn.silu(mixed).astype(jnp.bfloat16)


def surrogate_tail(hidden_block, middle_weight, out_weight):
    middle = jax.nn.silu(
        jnp.dot(hidden_block, middle_weight, preferred_element_type=jnp.float32)
    ).astype(jnp.bfloat16)
    return jnp.dot(middle, out_weight, preferred_element_type=jnp.float32)


def per_device(
    strain_rows,
    bands,
    damaged,
    owner,
    first_layers,
    middle_weight,
    out_weight,
    band_scale,
    back_weight,
):
    n_sec = lax.axis_size("sec")
    n_dev = lax.axis_size("dev")
    count_all = n_sec * n_dev
    list_rows = damaged.shape[0]
    slot_count = max(2, 2 * list_rows // count_all)
    group_slots = n_sec * slot_count
    feat_width = strain_rows.shape[1]
    hid = first_layers.shape[1]

    every_first = lax.all_gather(first_layers, "sec", axis=0, tiled=True).reshape(
        n_sec, feat_width, hid
    )
    parts = scale_parts(band_scale)

    features = jnp.take(strain_rows, damaged, axis=0)
    band_local = jnp.take(bands, damaged)
    target_owner = owner[:, 0]
    matches = (target_owner[:, None] == jnp.arange(count_all, dtype=jnp.int32)[None, :]).astype(
        jnp.int32
    )
    slot_rank = jnp.sum((jnp.cumsum(matches, axis=0) - 1) * matches, axis=1)
    owner_sec = target_owner // n_dev
    owner_dev = target_owner % n_dev
    target = owner_dev * group_slots + owner_sec * slot_count + slot_rank
    dispatch = (
        jnp.arange(n_dev * group_slots, dtype=jnp.int32)[:, None] == target[None, :]
    ).astype(jnp.bfloat16)
    packed = jnp.concatenate(
        [features, band_local.astype(jnp.bfloat16)[:, None]], axis=1
    )
    send = jnp.dot(dispatch, packed, preferred_element_type=jnp.float32).astype(jnp.bfloat16)
    send = send.reshape(1, n_dev, group_slots, feat_width + 1)
    send = jnp.broadcast_to(send, (n_sec, n_dev, group_slots, feat_width + 1)).reshape(
        count_all, group_slots, feat_width + 1
    )
    got = lax.all_to_all(send, ("sec", "dev"), split_axis=0, concat_axis=0, tiled=True)
    got = got.reshape(count_all, n_sec, slot_count, feat_width + 1).transpose(1, 0, 2, 3)
    got = got.reshape(n_sec, count_all * slot_count, feat_width + 1)
    rows = got[:, :, :feat_width]
    got_band = got[:, :, feat_width].astype(jnp.int32).reshape(-1)

    result = None
    for segment_index in range(PASSES):
        hidden = first_hidden(rows, every_first, got_band, parts)
        partial = surrogate_tail(hidden, middle_weight, out_weight)
        if segment_index + 1 < PASSES:
            values = lax.psum(partial, "sec").astype(jnp.bfloat16)
            rows = (
                rows.astype(jnp.float32)
                + jnp.dot(values, back_weight, preferred_element_type=jnp.float32).reshape(
                    rows.shape
                )
            ).astype(jnp.bfloat16)
        else:
            out_width = partial.shape[1]
            back = partial.reshape(n_sec, count_all, slot_count, out_width).transpose(1, 0, 2, 3)
            back = lax.all_to_all(back, ("sec", "dev"), split_axis=0, concat_axis=0, tiled=True)
            back = back.reshape(n_sec, n_dev * group_slots, out_width).sum(axis=0)
            result = jnp.take(back, target, axis=0).astype(jnp.bfloat16)
    return result


def solution(mesh):
    in_specs = (
        P(("sec", "dev"), None),
        P(("sec", "dev")),
        P(("sec", "dev")),
        P(("sec", "dev"), None),
        P(("sec", "dev"), None),
        P(None, "sec"),
        P("sec", None),
        P(),
        P(),
    )
    out_specs = P(("sec", "dev"), None)
    return jax.shard_map(
        per_device, mesh=mesh, in_specs=in_specs, out_specs=out_specs, check_vma=False
    )
```

```python
import jax
import jax.numpy as jnp
import numpy as np
from jax import lax
from jax.sharding import PartitionSpec as P

PASSES = 2


def scale_parts(band_scale):
    hi = band_scale.astype(jnp.bfloat16)
    rest = band_scale - hi.astype(jnp.float32)
    mid = rest.astype(jnp.bfloat16)
    lo = (rest - mid.astype(jnp.float32)).astype(jnp.bfloat16)
    return jnp.concatenate([hi, mid, lo], axis=0)


def band_rows(band_values, parts):
    levels = parts.shape[0] // 3
    level_ids = jnp.arange(3 * levels, dtype=jnp.int32) % levels
    picks = (band_values[:, None] == level_ids[None, :]).astype(jnp.bfloat16)
    return jnp.dot(picks, parts, preferred_element_type=jnp.float32)


def first_hidden(rows, weights, band_values, parts):
    mixed = jnp.einsum("srf,sfh->srh", rows, weights, preferred_element_type=jnp.float32)
    mixed = mixed.reshape(-1, weights.shape[2]) * band_rows(band_values, parts)
    return jax.nn.silu(mixed).astype(jnp.bfloat16)


def surrogate_tail(hidden_block, middle_weight, out_weight):
    middle = jax.nn.silu(
        jnp.dot(hidden_block, middle_weight, preferred_element_type=jnp.float32)
    ).astype(jnp.bfloat16)
    return jnp.dot(middle, out_weight, preferred_element_type=jnp.float32)


def xor_pairs(n, k):
    return [(i, i ^ k) for i in range(n)]


def per_device(
    strain_rows,
    bands,
    damaged,
    owner,
    first_layers,
    middle_weight,
    out_weight,
    band_scale,
    back_weight,
):
    n_sec = lax.axis_size("sec")
    n_dev = lax.axis_size("dev")
    assert n_sec & (n_sec - 1) == 0
    count_all = n_sec * n_dev
    list_rows = damaged.shape[0]
    slot_count = max(2, 2 * list_rows // count_all)
    group_slots = n_sec * slot_count
    feat_width = strain_rows.shape[1]

    block_first = [first_layers] + [
        lax.ppermute(first_layers, "sec", xor_pairs(n_sec, k)) for k in range(1, n_sec)
    ]
    parts = scale_parts(band_scale)

    features = jnp.take(strain_rows, damaged, axis=0)
    band_local = jnp.take(bands, damaged)
    target_owner = owner[:, 0]
    matches = (target_owner[:, None] == jnp.arange(count_all, dtype=jnp.int32)[None, :]).astype(
        jnp.int32
    )
    slot_rank = jnp.sum((jnp.cumsum(matches, axis=0) - 1) * matches, axis=1)
    owner_sec = target_owner // n_dev
    owner_dev = target_owner % n_dev
    target = owner_dev * group_slots + owner_sec * slot_count + slot_rank
    dispatch = (
        jnp.arange(n_dev * group_slots, dtype=jnp.int32)[:, None] == target[None, :]
    ).astype(jnp.bfloat16)
    packed = jnp.concatenate(
        [features, band_local.astype(jnp.bfloat16)[:, None]], axis=1
    )
    grp = jnp.dot(dispatch, packed, preferred_element_type=jnp.float32).astype(jnp.bfloat16)
    grp = grp.reshape(n_dev, n_sec, slot_count, feat_width + 1)
    xor_table = np.bitwise_xor.outer(np.arange(n_sec), np.arange(n_sec)).reshape(-1)
    send = jnp.take(grp, jnp.asarray(xor_table, jnp.int32), axis=1)
    send = send.reshape(n_dev, n_sec, n_sec, slot_count, feat_width + 1).transpose(1, 0, 2, 3, 4)
    send = send.reshape(count_all, group_slots, feat_width + 1)
    got = lax.all_to_all(send, ("sec", "dev"), split_axis=0, concat_axis=0, tiled=True)
    got = got.reshape(count_all, n_sec, slot_count, feat_width + 1).transpose(1, 0, 2, 3)
    got = got.reshape(n_sec, count_all * slot_count, feat_width + 1)
    rows = [got[k, :, :feat_width] for k in range(n_sec)]
    got_band = [got[k, :, feat_width].astype(jnp.int32) for k in range(n_sec)]

    result = None
    for segment_index in range(PASSES):
        partial = []
        for k in range(n_sec):
            hidden = first_hidden(rows[k][None], block_first[k][None], got_band[k], parts)
            partial.append(surrogate_tail(hidden, middle_weight, out_weight))
        own_sum = partial[0]
        for k in range(1, n_sec):
            own_sum = own_sum + lax.ppermute(partial[k], "sec", xor_pairs(n_sec, k))
        own_values = own_sum.astype(jnp.bfloat16)
        if segment_index + 1 < PASSES:
            values = [own_values] + [
                lax.ppermute(own_values, "sec", xor_pairs(n_sec, k)) for k in range(1, n_sec)
            ]
            rows = [
                (
                    rows[k].astype(jnp.float32)
                    + jnp.dot(values[k], back_weight, preferred_element_type=jnp.float32)
                ).astype(jnp.bfloat16)
                for k in range(n_sec)
            ]
        else:
            out_width = own_values.shape[1]
            back = lax.all_to_all(
                own_values.reshape(count_all, slot_count, out_width),
                ("sec", "dev"),
                split_axis=0,
                concat_axis=0,
                tiled=True,
            )
            home = target_owner * slot_count + slot_rank
            result = jnp.take(back.reshape(count_all * slot_count, out_width), home, axis=0)
    return result


def solution(mesh):
    in_specs = (
        P(("sec", "dev"), None),
        P(("sec", "dev")),
        P(("sec", "dev")),
        P(("sec", "dev"), None),
        P(("sec", "dev"), None),
        P(None, "sec"),
        P("sec", None),
        P(),
        P(),
    )
    out_specs = P(("sec", "dev"), None)
    return jax.shard_map(
        per_device, mesh=mesh, in_specs=in_specs, out_specs=out_specs, check_vma=False
    )
```

```python
import jax
import jax.numpy as jnp
import numpy as np
from jax import lax
from jax.sharding import PartitionSpec as P

PASSES = 2


def scale_parts(band_scale):
    hi = band_scale.astype(jnp.bfloat16)
    rest = band_scale - hi.astype(jnp.float32)
    mid = rest.astype(jnp.bfloat16)
    lo = (rest - mid.astype(jnp.float32)).astype(jnp.bfloat16)
    return jnp.concatenate([hi, mid, lo], axis=0)


def band_rows(band_values, parts):
    levels = parts.shape[0] // 3
    level_ids = jnp.arange(3 * levels, dtype=jnp.int32) % levels
    picks = (band_values[:, None] == level_ids[None, :]).astype(jnp.bfloat16)
    return jnp.dot(picks, parts, preferred_element_type=jnp.float32)


def first_hidden(rows, weights, band_values, parts):
    mixed = jnp.einsum("srf,sfh->srh", rows, weights, preferred_element_type=jnp.float32)
    mixed = mixed.reshape(-1, weights.shape[2]) * band_rows(band_values, parts)
    return jax.nn.silu(mixed).astype(jnp.bfloat16)


def surrogate_tail(hidden_block, middle_weight, out_weight):
    middle = jax.nn.silu(
        jnp.dot(hidden_block, middle_weight, preferred_element_type=jnp.float32)
    ).astype(jnp.bfloat16)
    return jnp.dot(middle, out_weight, preferred_element_type=jnp.float32)


def xor_pairs(n, k):
    return [(i, i ^ k) for i in range(n)]


def per_device(
    strain_rows,
    bands,
    damaged,
    owner,
    first_layers,
    middle_weight,
    out_weight,
    band_scale,
    back_weight,
):
    n_sec = lax.axis_size("sec")
    n_dev = lax.axis_size("dev")
    assert n_sec & (n_sec - 1) == 0
    count_all = n_sec * n_dev
    list_rows = damaged.shape[0]
    slot_count = max(2, 2 * list_rows // count_all)
    group_slots = n_sec * slot_count
    feat_width = strain_rows.shape[1]

    block_first = [first_layers] + [
        lax.ppermute(first_layers, "sec", xor_pairs(n_sec, k)) for k in range(1, n_sec)
    ]
    parts = scale_parts(band_scale)

    features = jnp.take(strain_rows, damaged, axis=0)
    band_local = jnp.take(bands, damaged)
    target_owner = owner[:, 0]
    matches = (target_owner[:, None] == jnp.arange(count_all, dtype=jnp.int32)[None, :]).astype(
        jnp.int32
    )
    slot_rank = jnp.sum((jnp.cumsum(matches, axis=0) - 1) * matches, axis=1)
    owner_sec = target_owner // n_dev
    owner_dev = target_owner % n_dev
    target = owner_dev * group_slots + owner_sec * slot_count + slot_rank
    dispatch = (
        jnp.arange(n_dev * group_slots, dtype=jnp.int32)[:, None] == target[None, :]
    ).astype(jnp.bfloat16)
    packed = jnp.concatenate(
        [features, band_local.astype(jnp.bfloat16)[:, None]], axis=1
    )
    grp = jnp.dot(dispatch, packed, preferred_element_type=jnp.float32).astype(jnp.bfloat16)
    grp = grp.reshape(n_dev, n_sec, slot_count, feat_width + 1)
    xor_table = np.bitwise_xor.outer(np.arange(n_sec), np.arange(n_sec)).reshape(-1)
    send = jnp.take(grp, jnp.asarray(xor_table, jnp.int32), axis=1)
    send = send.reshape(n_dev, n_sec, n_sec, slot_count, feat_width + 1).transpose(1, 0, 2, 3, 4)
    send = send.reshape(count_all, group_slots, feat_width + 1)
    got = lax.all_to_all(send, ("sec", "dev"), split_axis=0, concat_axis=0, tiled=True)
    got = got.reshape(count_all, n_sec, slot_count, feat_width + 1).transpose(1, 0, 2, 3)
    got = got.reshape(n_sec, count_all * slot_count, feat_width + 1)
    rows = [got[k, :, :feat_width] for k in range(n_sec)]
    got_band = [got[k, :, feat_width].astype(jnp.int32) for k in range(n_sec)]

    result = None
    for segment_index in range(PASSES):
        partial = []
        for k in range(n_sec):
            hidden = lax.optimization_barrier(
                first_hidden(rows[k][None], block_first[k][None], got_band[k], parts)
            )
            partial.append(surrogate_tail(hidden, middle_weight, out_weight))
        own_sum = partial[0]
        for k in range(1, n_sec):
            own_sum = own_sum + lax.ppermute(partial[k], "sec", xor_pairs(n_sec, k))
        own_values = own_sum.astype(jnp.bfloat16)
        if segment_index + 1 < PASSES:
            values = [own_values] + [
                lax.ppermute(own_values, "sec", xor_pairs(n_sec, k)) for k in range(1, n_sec)
            ]
            rows = [
                (
                    rows[k].astype(jnp.float32)
                    + jnp.dot(values[k], back_weight, preferred_element_type=jnp.float32)
                ).astype(jnp.bfloat16)
                for k in range(n_sec)
            ]
        else:
            out_width = own_values.shape[1]
            back = lax.all_to_all(
                own_values.reshape(count_all, slot_count, out_width),
                ("sec", "dev"),
                split_axis=0,
                concat_axis=0,
                tiled=True,
            )
            home = target_owner * slot_count + slot_rank
            result = jnp.take(back.reshape(count_all * slot_count, out_width), home, axis=0)
    return result


def solution(mesh):
    in_specs = (
        P(("sec", "dev"), None),
        P(("sec", "dev")),
        P(("sec", "dev")),
        P(("sec", "dev"), None),
        P(("sec", "dev"), None),
        P(None, "sec"),
        P("sec", None),
        P(),
        P(),
    )
    out_specs = P(("sec", "dev"), None)
    return jax.shard_map(
        per_device, mesh=mesh, in_specs=in_specs, out_specs=out_specs, check_vma=False
    )
```

```python
import jax
import jax.numpy as jnp
import numpy as np
from jax import lax
from jax.sharding import PartitionSpec as P

PASSES = 2


def scale_parts(band_scale):
    hi = band_scale.astype(jnp.bfloat16)
    rest = band_scale - hi.astype(jnp.float32)
    mid = rest.astype(jnp.bfloat16)
    lo = (rest - mid.astype(jnp.float32)).astype(jnp.bfloat16)
    return jnp.concatenate([hi, mid, lo], axis=0)


def band_rows(band_values, parts):
    levels = parts.shape[0] // 3
    level_ids = jnp.arange(3 * levels, dtype=jnp.int32) % levels
    picks = (band_values[:, None] == level_ids[None, :]).astype(jnp.bfloat16)
    return jnp.dot(picks, parts, preferred_element_type=jnp.float32)


def first_hidden(rows, weights, band_values, parts):
    mixed = jnp.einsum("srf,sfh->srh", rows, weights, preferred_element_type=jnp.float32)
    mixed = mixed.reshape(-1, weights.shape[2]) * band_rows(band_values, parts)
    return jax.nn.silu(mixed).astype(jnp.bfloat16)


def surrogate_tail(hidden_block, middle_weight, out_weight):
    middle = jax.nn.silu(
        jnp.dot(hidden_block, middle_weight, preferred_element_type=jnp.float32)
    ).astype(jnp.bfloat16)
    return jnp.dot(middle, out_weight, preferred_element_type=jnp.float32)


def xor_pairs(n, k):
    return [(i, i ^ k) for i in range(n)]


def per_device(
    strain_rows,
    bands,
    damaged,
    owner,
    first_layers,
    middle_weight,
    out_weight,
    band_scale,
    back_weight,
):
    n_sec = lax.axis_size("sec")
    n_dev = lax.axis_size("dev")
    assert n_sec & (n_sec - 1) == 0
    count_all = n_sec * n_dev
    list_rows = damaged.shape[0]
    slot_count = max(2, 2 * list_rows // count_all)
    group_slots = n_sec * slot_count
    feat_width = strain_rows.shape[1]

    block_first = [first_layers] + [
        lax.ppermute(first_layers, "sec", xor_pairs(n_sec, k)) for k in range(1, n_sec)
    ]
    parts = scale_parts(band_scale)

    features = jnp.take(strain_rows, damaged, axis=0)
    band_local = jnp.take(bands, damaged)
    target_owner = owner[:, 0]
    matches = (target_owner[:, None] == jnp.arange(count_all, dtype=jnp.int32)[None, :]).astype(
        jnp.int32
    )
    slot_rank = jnp.sum((jnp.cumsum(matches, axis=0) - 1) * matches, axis=1)
    owner_sec = target_owner // n_dev
    owner_dev = target_owner % n_dev
    target = owner_dev * group_slots + owner_sec * slot_count + slot_rank
    dispatch = (
        jnp.arange(n_dev * group_slots, dtype=jnp.int32)[:, None] == target[None, :]
    ).astype(jnp.bfloat16)
    packed = jnp.concatenate(
        [features, band_local.astype(jnp.bfloat16)[:, None]], axis=1
    )
    grp = jnp.dot(dispatch, packed, preferred_element_type=jnp.float32).astype(jnp.bfloat16)
    grp = grp.reshape(n_dev, n_sec, slot_count, feat_width + 1)
    xor_table = np.bitwise_xor.outer(np.arange(n_sec), np.arange(n_sec)).reshape(-1)
    send = jnp.take(grp, jnp.asarray(xor_table, jnp.int32), axis=1)
    send = send.reshape(n_dev, n_sec, n_sec, slot_count, feat_width + 1).transpose(1, 0, 2, 3, 4)
    send = send.reshape(count_all, group_slots, feat_width + 1)
    got = lax.all_to_all(send, ("sec", "dev"), split_axis=0, concat_axis=0, tiled=True)
    got = got.reshape(count_all, n_sec, slot_count, feat_width + 1).transpose(1, 0, 2, 3)
    got = got.reshape(n_sec, count_all * slot_count, feat_width + 1)
    rows = got[:, :, :feat_width]
    got_band = got[:, :, feat_width].astype(jnp.int32).reshape(-1)
    every_first = jnp.stack(block_first)

    result = None
    for segment_index in range(PASSES):
        hidden = first_hidden(rows, every_first, got_band, parts)
        partial = surrogate_tail(hidden, middle_weight, out_weight).reshape(
            n_sec, rows.shape[1], -1
        )
        own_sum = partial[0]
        for k in range(1, n_sec):
            own_sum = own_sum + lax.ppermute(partial[k], "sec", xor_pairs(n_sec, k))
        own_values = own_sum.astype(jnp.bfloat16)
        if segment_index + 1 < PASSES:
            values = jnp.stack(
                [own_values]
                + [lax.ppermute(own_values, "sec", xor_pairs(n_sec, k)) for k in range(1, n_sec)]
            )
            rows = (
                rows.astype(jnp.float32)
                + jnp.einsum("sro,of->srf", values, back_weight, preferred_element_type=jnp.float32)
            ).astype(jnp.bfloat16)
        else:
            out_width = own_values.shape[1]
            back = lax.all_to_all(
                own_values.reshape(count_all, slot_count, out_width),
                ("sec", "dev"),
                split_axis=0,
                concat_axis=0,
                tiled=True,
            )
            home = target_owner * slot_count + slot_rank
            result = jnp.take(back.reshape(count_all * slot_count, out_width), home, axis=0)
    return result


def solution(mesh):
    in_specs = (
        P(("sec", "dev"), None),
        P(("sec", "dev")),
        P(("sec", "dev")),
        P(("sec", "dev"), None),
        P(("sec", "dev"), None),
        P(None, "sec"),
        P("sec", None),
        P(),
        P(),
    )
    out_specs = P(("sec", "dev"), None)
    return jax.shard_map(
        per_device, mesh=mesh, in_specs=in_specs, out_specs=out_specs, check_vma=False
    )
```

```python
import jax
import jax.numpy as jnp
import numpy as np
from jax import lax
from jax.experimental import pallas as pl
from jax.sharding import PartitionSpec as P

PASSES = 2


def scale_parts(band_scale):
    hi = band_scale.astype(jnp.bfloat16)
    rest = band_scale - hi.astype(jnp.float32)
    mid = rest.astype(jnp.bfloat16)
    lo = (rest - mid.astype(jnp.float32)).astype(jnp.bfloat16)
    return jnp.concatenate([hi, mid, lo], axis=0)


def band_picks(band_values, parts):
    levels = parts.shape[0] // 3
    level_ids = jnp.arange(3 * levels, dtype=jnp.int32) % levels
    return (band_values[..., None] == level_ids).astype(jnp.bfloat16)


def first_kernel(x_ref, w_ref, p_ref, s_ref, o_ref):
    mixed = jnp.dot(x_ref[...], w_ref[...], preferred_element_type=jnp.float32)
    scale = jnp.dot(p_ref[...], s_ref[...], preferred_element_type=jnp.float32)
    v = mixed * scale
    o_ref[...] = (v / (1.0 + jnp.exp(-v))).astype(o_ref.dtype)


def first_hidden(rows, weights, picks, parts, interpret=False):
    n_blocks, n_rows, feat = rows.shape
    hid = weights.shape[2]
    n_pick = picks.shape[2]
    row_tile = min(n_rows, 256)
    col_tile = min(hid, 512)
    row_steps = n_rows // row_tile
    return pl.pallas_call(
        first_kernel,
        grid=(n_blocks, row_steps, hid // col_tile),
        in_specs=[
            pl.BlockSpec((None, row_tile, feat), lambda s, i, j: (s, i, 0)),
            pl.BlockSpec((None, feat, col_tile), lambda s, i, j: (s, 0, j)),
            pl.BlockSpec((None, row_tile, n_pick), lambda s, i, j: (s, i, 0)),
            pl.BlockSpec((n_pick, col_tile), lambda s, i, j: (0, j)),
        ],
        out_specs=pl.BlockSpec((row_tile, col_tile), lambda s, i, j: (s * row_steps + i, j)),
        out_shape=jax.ShapeDtypeStruct((n_blocks * n_rows, hid), jnp.bfloat16),
        cost_estimate=pl.CostEstimate(
            flops=2 * n_blocks * n_rows * hid * (feat + n_pick),
            transcendentals=n_blocks * n_rows * hid,
            bytes_accessed=2 * (n_blocks * n_rows * hid + n_blocks * feat * hid * row_steps),
        ),
        interpret=interpret,
    )(rows, weights, picks, parts)


def surrogate_tail(hidden_block, middle_weight, out_weight):
    middle = jax.nn.silu(
        jnp.dot(hidden_block, middle_weight, preferred_element_type=jnp.float32)
    ).astype(jnp.bfloat16)
    return jnp.dot(middle, out_weight, preferred_element_type=jnp.float32)


def xor_pairs(n, k):
    return [(i, i ^ k) for i in range(n)]


def per_device(
    strain_rows,
    bands,
    damaged,
    owner,
    first_layers,
    middle_weight,
    out_weight,
    band_scale,
    back_weight,
):
    n_sec = lax.axis_size("sec")
    n_dev = lax.axis_size("dev")
    assert n_sec & (n_sec - 1) == 0
    count_all = n_sec * n_dev
    list_rows = damaged.shape[0]
    slot_count = max(2, 2 * list_rows // count_all)
    group_slots = n_sec * slot_count
    feat_width = strain_rows.shape[1]

    block_first = [first_layers] + [
        lax.ppermute(first_layers, "sec", xor_pairs(n_sec, k)) for k in range(1, n_sec)
    ]
    parts = scale_parts(band_scale)

    features = jnp.take(strain_rows, damaged, axis=0)
    band_local = jnp.take(bands, damaged)
    target_owner = owner[:, 0]
    matches = (target_owner[:, None] == jnp.arange(count_all, dtype=jnp.int32)[None, :]).astype(
        jnp.int32
    )
    slot_rank = jnp.sum((jnp.cumsum(matches, axis=0) - 1) * matches, axis=1)
    owner_sec = target_owner // n_dev
    owner_dev = target_owner % n_dev
    target = owner_dev * group_slots + owner_sec * slot_count + slot_rank
    dispatch = (
        jnp.arange(n_dev * group_slots, dtype=jnp.int32)[:, None] == target[None, :]
    ).astype(jnp.bfloat16)
    packed = jnp.concatenate(
        [features, band_local.astype(jnp.bfloat16)[:, None]], axis=1
    )
    grp = jnp.dot(dispatch, packed, preferred_element_type=jnp.float32).astype(jnp.bfloat16)
    grp = grp.reshape(n_dev, n_sec, slot_count, feat_width + 1)
    xor_table = np.bitwise_xor.outer(np.arange(n_sec), np.arange(n_sec)).reshape(-1)
    send = jnp.take(grp, jnp.asarray(xor_table, jnp.int32), axis=1)
    send = send.reshape(n_dev, n_sec, n_sec, slot_count, feat_width + 1).transpose(1, 0, 2, 3, 4)
    send = send.reshape(count_all, group_slots, feat_width + 1)
    got = lax.all_to_all(send, ("sec", "dev"), split_axis=0, concat_axis=0, tiled=True)
    got = got.reshape(count_all, n_sec, slot_count, feat_width + 1).transpose(1, 0, 2, 3)
    got = got.reshape(n_sec, count_all * slot_count, feat_width + 1)
    rows = got[:, :, :feat_width]
    picks = band_picks(got[:, :, feat_width].astype(jnp.int32), parts)
    every_first = jnp.stack(block_first)

    result = None
    for segment_index in range(PASSES):
        hidden = first_hidden(rows, every_first, picks, parts)
        partial = surrogate_tail(hidden, middle_weight, out_weight).reshape(
            n_sec, rows.shape[1], -1
        )
        own_sum = partial[0]
        for k in range(1, n_sec):
            own_sum = own_sum + lax.ppermute(partial[k], "sec", xor_pairs(n_sec, k))
        own_values = own_sum.astype(jnp.bfloat16)
        if segment_index + 1 < PASSES:
            values = jnp.stack(
                [own_values]
                + [lax.ppermute(own_values, "sec", xor_pairs(n_sec, k)) for k in range(1, n_sec)]
            )
            rows = (
                rows.astype(jnp.float32)
                + jnp.einsum("sro,of->srf", values, back_weight, preferred_element_type=jnp.float32)
            ).astype(jnp.bfloat16)
        else:
            out_width = own_values.shape[1]
            back = lax.all_to_all(
                own_values.reshape(count_all, slot_count, out_width),
                ("sec", "dev"),
                split_axis=0,
                concat_axis=0,
                tiled=True,
            )
            home = target_owner * slot_count + slot_rank
            result = jnp.take(back.reshape(count_all * slot_count, out_width), home, axis=0)
    return result


def solution(mesh):
    in_specs = (
        P(("sec", "dev"), None),
        P(("sec", "dev")),
        P(("sec", "dev")),
        P(("sec", "dev"), None),
        P(("sec", "dev"), None),
        P(None, "sec"),
        P("sec", None),
        P(),
        P(),
    )
    out_specs = P(("sec", "dev"), None)
    return jax.shard_map(
        per_device, mesh=mesh, in_specs=in_specs, out_specs=out_specs, check_vma=False
    )
```

```python
import jax
import jax.numpy as jnp
import numpy as np
from jax import lax
from jax.experimental import pallas as pl
from jax.sharding import PartitionSpec as P

PASSES = 2


def scale_parts(band_scale):
    hi = band_scale.astype(jnp.bfloat16)
    rest = band_scale - hi.astype(jnp.float32)
    mid = rest.astype(jnp.bfloat16)
    lo = (rest - mid.astype(jnp.float32)).astype(jnp.bfloat16)
    return jnp.concatenate([hi, mid, lo], axis=0)


def band_picks(band_values, parts):
    levels = parts.shape[0] // 3
    level_ids = jnp.arange(3 * levels, dtype=jnp.int32) % levels
    return (band_values[..., None] == level_ids).astype(jnp.bfloat16)


def first_kernel(x_ref, *refs):
    w_refs, (p_ref, s_ref, o_ref) = refs[:-3], refs[-3:]
    block = pl.program_id(0)
    for k, w_ref in enumerate(w_refs):

        @pl.when(block == k)
        def _():
            mixed = jnp.dot(x_ref[...], w_ref[...], preferred_element_type=jnp.float32)
            scale = jnp.dot(p_ref[...], s_ref[...], preferred_element_type=jnp.float32)
            v = mixed * scale
            o_ref[...] = (v * jax.nn.sigmoid(v)).astype(o_ref.dtype)


def weight_spec(k, feat, col_tile, col_steps):
    def index(s, i, j):
        return (0, jnp.where(s == k, j, jnp.where(s < k, 0, col_steps - 1)))

    return pl.BlockSpec((feat, col_tile), index)


def first_hidden(rows, weights, picks, parts, interpret=False):
    n_blocks, n_rows, feat = rows.shape
    hid = weights[0].shape[1]
    n_pick = picks.shape[2]
    row_tile = min(n_rows, 256)
    col_tile = min(hid, 4096)
    row_steps = n_rows // row_tile
    col_steps = hid // col_tile
    return pl.pallas_call(
        first_kernel,
        grid=(n_blocks, row_steps, col_steps),
        in_specs=[pl.BlockSpec((None, row_tile, feat), lambda s, i, j: (s, i, 0))]
        + [weight_spec(k, feat, col_tile, col_steps) for k in range(n_blocks)]
        + [
            pl.BlockSpec((None, row_tile, n_pick), lambda s, i, j: (s, i, 0)),
            pl.BlockSpec((n_pick, col_tile), lambda s, i, j: (0, j)),
        ],
        out_specs=pl.BlockSpec((row_tile, col_tile), lambda s, i, j: (s * row_steps + i, j)),
        out_shape=jax.ShapeDtypeStruct((n_blocks * n_rows, hid), jnp.bfloat16),
        cost_estimate=pl.CostEstimate(
            flops=2 * n_blocks * n_rows * hid * (feat + n_pick),
            transcendentals=n_blocks * n_rows * hid,
            bytes_accessed=2 * (n_blocks * n_rows * hid + n_blocks * feat * hid * row_steps),
        ),
        interpret=interpret,
    )(rows, *weights, picks, parts)


def surrogate_tail(hidden_block, middle_weight, out_weight):
    middle = jax.nn.silu(
        jnp.dot(hidden_block, middle_weight, preferred_element_type=jnp.float32)
    ).astype(jnp.bfloat16)
    return jnp.dot(middle, out_weight, preferred_element_type=jnp.float32)


def xor_pairs(n, k):
    return [(i, i ^ k) for i in range(n)]


def per_device(
    strain_rows,
    bands,
    damaged,
    owner,
    first_layers,
    middle_weight,
    out_weight,
    band_scale,
    back_weight,
):
    n_sec = lax.axis_size("sec")
    n_dev = lax.axis_size("dev")
    assert n_sec & (n_sec - 1) == 0
    count_all = n_sec * n_dev
    list_rows = damaged.shape[0]
    slot_count = max(2, 2 * list_rows // count_all)
    group_slots = n_sec * slot_count
    feat_width = strain_rows.shape[1]

    block_first = [first_layers] + [
        lax.ppermute(first_layers, "sec", xor_pairs(n_sec, k)) for k in range(1, n_sec)
    ]
    parts = scale_parts(band_scale)

    features = jnp.take(strain_rows, damaged, axis=0)
    band_local = jnp.take(bands, damaged)
    target_owner = owner[:, 0]
    matches = (target_owner[:, None] == jnp.arange(count_all, dtype=jnp.int32)[None, :]).astype(
        jnp.int32
    )
    slot_rank = jnp.sum((jnp.cumsum(matches, axis=0) - 1) * matches, axis=1)
    owner_sec = target_owner // n_dev
    owner_dev = target_owner % n_dev
    target = owner_dev * group_slots + owner_sec * slot_count + slot_rank
    dispatch = (
        jnp.arange(n_dev * group_slots, dtype=jnp.int32)[:, None] == target[None, :]
    ).astype(jnp.bfloat16)
    packed = jnp.concatenate(
        [features, band_local.astype(jnp.bfloat16)[:, None]], axis=1
    )
    grp = jnp.dot(dispatch, packed, preferred_element_type=jnp.float32).astype(jnp.bfloat16)
    grp = grp.reshape(n_dev, n_sec, slot_count, feat_width + 1)
    xor_table = np.bitwise_xor.outer(np.arange(n_sec), np.arange(n_sec)).reshape(-1)
    send = jnp.take(grp, jnp.asarray(xor_table, jnp.int32), axis=1)
    send = send.reshape(n_dev, n_sec, n_sec, slot_count, feat_width + 1).transpose(1, 0, 2, 3, 4)
    send = send.reshape(count_all, group_slots, feat_width + 1)
    got = lax.all_to_all(send, ("sec", "dev"), split_axis=0, concat_axis=0, tiled=True)
    got = got.reshape(count_all, n_sec, slot_count, feat_width + 1).transpose(1, 0, 2, 3)
    got = got.reshape(n_sec, count_all * slot_count, feat_width + 1)
    rows = got[:, :, :feat_width]
    picks = band_picks(got[:, :, feat_width].astype(jnp.int32), parts)

    result = None
    for segment_index in range(PASSES):
        hidden = first_hidden(rows, block_first, picks, parts)
        partial = surrogate_tail(hidden, middle_weight, out_weight).reshape(
            n_sec, rows.shape[1], -1
        )
        own_sum = partial[0]
        for k in range(1, n_sec):
            own_sum = own_sum + lax.ppermute(partial[k], "sec", xor_pairs(n_sec, k))
        own_values = own_sum.astype(jnp.bfloat16)
        if segment_index + 1 < PASSES:
            values = jnp.stack(
                [own_values]
                + [lax.ppermute(own_values, "sec", xor_pairs(n_sec, k)) for k in range(1, n_sec)]
            )
            rows = (
                rows.astype(jnp.float32)
                + jnp.einsum("sro,of->srf", values, back_weight, preferred_element_type=jnp.float32)
            ).astype(jnp.bfloat16)
        else:
            out_width = own_values.shape[1]
            back = lax.all_to_all(
                own_values.reshape(count_all, slot_count, out_width),
                ("sec", "dev"),
                split_axis=0,
                concat_axis=0,
                tiled=True,
            )
            home = target_owner * slot_count + slot_rank
            result = jnp.take(back.reshape(count_all * slot_count, out_width), home, axis=0)
    return result


def solution(mesh):
    in_specs = (
        P(("sec", "dev"), None),
        P(("sec", "dev")),
        P(("sec", "dev")),
        P(("sec", "dev"), None),
        P(("sec", "dev"), None),
        P(None, "sec"),
        P("sec", None),
        P(),
        P(),
    )
    out_specs = P(("sec", "dev"), None)
    return jax.shard_map(
        per_device, mesh=mesh, in_specs=in_specs, out_specs=out_specs, check_vma=False
    )
```

```python
import jax
import jax.numpy as jnp
import numpy as np
from jax import lax
from jax.experimental import pallas as pl
from jax.sharding import PartitionSpec as P

PASSES = 2


def scale_parts(band_scale):
    hi = band_scale.astype(jnp.bfloat16)
    rest = band_scale - hi.astype(jnp.float32)
    mid = rest.astype(jnp.bfloat16)
    lo = (rest - mid.astype(jnp.float32)).astype(jnp.bfloat16)
    return jnp.concatenate([hi, mid, lo], axis=0)


def band_picks(band_values, parts):
    levels = parts.shape[0] // 3
    level_ids = jnp.arange(3 * levels, dtype=jnp.int32) % levels
    return (band_values[..., None] == level_ids).astype(jnp.bfloat16)


def first_kernel(x_ref, *refs):
    w_refs, (p_ref, s_ref, o_ref) = refs[:-3], refs[-3:]
    block = pl.program_id(0)
    for k, w_ref in enumerate(w_refs):

        @pl.when(block == k)
        def _():
            mixed = jnp.dot(x_ref[...], w_ref[...], preferred_element_type=jnp.float32)
            scale = jnp.dot(p_ref[...], s_ref[...], preferred_element_type=jnp.float32)
            v = mixed * scale
            o_ref[...] = (v * jax.nn.sigmoid(v)).astype(o_ref.dtype)


def weight_spec(k, feat, col_tile, col_steps):
    def index(s, i, j):
        return (0, jnp.where(s == k, j, jnp.where(s < k, 0, col_steps - 1)))

    return pl.BlockSpec((feat, col_tile), index)


def first_hidden(rows, weights, picks, parts, interpret=False):
    n_blocks, n_rows, feat = rows.shape
    hid = weights[0].shape[1]
    n_pick = picks.shape[2]
    row_tile = min(n_rows, 256)
    col_tile = min(hid, 4096)
    row_steps = n_rows // row_tile
    col_steps = hid // col_tile
    return pl.pallas_call(
        first_kernel,
        grid=(n_blocks, row_steps, col_steps),
        in_specs=[pl.BlockSpec((None, row_tile, feat), lambda s, i, j: (s, i, 0))]
        + [weight_spec(k, feat, col_tile, col_steps) for k in range(n_blocks)]
        + [
            pl.BlockSpec((None, row_tile, n_pick), lambda s, i, j: (s, i, 0)),
            pl.BlockSpec((n_pick, col_tile), lambda s, i, j: (0, j)),
        ],
        out_specs=pl.BlockSpec((row_tile, col_tile), lambda s, i, j: (s * row_steps + i, j)),
        out_shape=jax.ShapeDtypeStruct((n_blocks * n_rows, hid), jnp.bfloat16),
        cost_estimate=pl.CostEstimate(
            flops=2 * n_blocks * n_rows * hid * (feat + n_pick),
            transcendentals=n_blocks * n_rows * hid,
            bytes_accessed=2 * (n_blocks * n_rows * hid + n_blocks * feat * hid * row_steps),
        ),
        interpret=interpret,
    )(rows, *weights, picks, parts)


def surrogate_tail(hidden_block, middle_weight, out_weight):
    middle = jax.nn.silu(
        jnp.dot(hidden_block, middle_weight, preferred_element_type=jnp.float32)
    ).astype(jnp.bfloat16)
    return jnp.dot(middle, out_weight, preferred_element_type=jnp.float32)


def xor_pairs(n, k):
    return [(i, i ^ k) for i in range(n)]


def realign(block, k, n_sec):
    order = np.bitwise_xor(np.arange(n_sec), k)
    return block.reshape(n_sec, -1, block.shape[-1])[order].reshape(block.shape)


def per_device(
    strain_rows,
    bands,
    damaged,
    owner,
    first_layers,
    middle_weight,
    out_weight,
    band_scale,
    back_weight,
):
    n_sec = lax.axis_size("sec")
    n_dev = lax.axis_size("dev")
    assert n_sec & (n_sec - 1) == 0
    count_all = n_sec * n_dev
    list_rows = damaged.shape[0]
    slot_count = max(2, 2 * list_rows // count_all)
    group_slots = n_sec * slot_count
    feat_width = strain_rows.shape[1]

    block_first = [first_layers] + [
        lax.ppermute(first_layers, "sec", xor_pairs(n_sec, k)) for k in range(1, n_sec)
    ]
    parts = scale_parts(band_scale)

    features = jnp.take(strain_rows, damaged, axis=0)
    band_local = jnp.take(bands, damaged)
    target_owner = owner[:, 0]
    matches = (target_owner[:, None] == jnp.arange(count_all, dtype=jnp.int32)[None, :]).astype(
        jnp.int32
    )
    slot_rank = jnp.sum((jnp.cumsum(matches, axis=0) - 1) * matches, axis=1)
    owner_sec = target_owner // n_dev
    owner_dev = target_owner % n_dev
    target = owner_dev * group_slots + owner_sec * slot_count + slot_rank
    dispatch = (
        jnp.arange(n_dev * group_slots, dtype=jnp.int32)[:, None] == target[None, :]
    ).astype(jnp.bfloat16)
    packed = jnp.concatenate(
        [features, band_local.astype(jnp.bfloat16)[:, None]], axis=1
    )
    grp = jnp.dot(dispatch, packed, preferred_element_type=jnp.float32).astype(jnp.bfloat16)
    my_sec = lax.axis_index("sec")
    sec_turn = jnp.bitwise_xor(jnp.arange(n_sec, dtype=jnp.int32), my_sec)
    grp = grp.reshape(n_dev, group_slots, feat_width + 1)
    got_dev = lax.all_to_all(grp, "dev", split_axis=0, concat_axis=0, tiled=True)
    pieces = [got_dev] + [
        lax.ppermute(got_dev, "sec", xor_pairs(n_sec, j)) for j in range(1, n_sec)
    ]
    got = jnp.stack(pieces).reshape(n_sec, n_dev, n_sec, slot_count, feat_width + 1)
    got = jnp.take(got, sec_turn, axis=2).transpose(2, 0, 1, 3, 4)
    got = got.reshape(n_sec, n_sec * n_dev * slot_count, feat_width + 1)
    rows = got[:, :, :feat_width]
    picks = band_picks(got[:, :, feat_width].astype(jnp.int32), parts)

    result = None
    for segment_index in range(PASSES):
        hidden = first_hidden(rows, block_first, picks, parts)
        partial = surrogate_tail(hidden, middle_weight, out_weight).reshape(
            n_sec, rows.shape[1], -1
        )
        own_sum = partial[0]
        for k in range(1, n_sec):
            own_sum = own_sum + realign(
                lax.ppermute(partial[k], "sec", xor_pairs(n_sec, k)), k, n_sec
            )
        own_values = own_sum.astype(jnp.bfloat16)
        if segment_index + 1 < PASSES:
            values = jnp.stack(
                [own_values]
                + [
                    realign(lax.ppermute(own_values, "sec", xor_pairs(n_sec, k)), k, n_sec)
                    for k in range(1, n_sec)
                ]
            )
            rows = (
                rows.astype(jnp.float32)
                + jnp.einsum("sro,of->srf", values, back_weight, preferred_element_type=jnp.float32)
            ).astype(jnp.bfloat16)
        else:
            out_width = own_values.shape[1]
            back = jnp.take(own_values.reshape(n_sec, -1, out_width), sec_turn, axis=0)
            back = lax.all_to_all(
                back.reshape(count_all, slot_count, out_width),
                ("sec", "dev"),
                split_axis=0,
                concat_axis=0,
                tiled=True,
            )
            home = target_owner * slot_count + slot_rank
            result = jnp.take(back.reshape(count_all * slot_count, out_width), home, axis=0)
    return result


def solution(mesh):
    in_specs = (
        P(("sec", "dev"), None),
        P(("sec", "dev")),
        P(("sec", "dev")),
        P(("sec", "dev"), None),
        P(("sec", "dev"), None),
        P(None, "sec"),
        P("sec", None),
        P(),
        P(),
    )
    out_specs = P(("sec", "dev"), None)
    return jax.shard_map(
        per_device, mesh=mesh, in_specs=in_specs, out_specs=out_specs, check_vma=False
    )
```

```python
import functools

import jax
import jax.numpy as jnp
import numpy as np
from jax import lax
from jax.experimental import pallas as pl
from jax.experimental.pallas import tpu as pltpu
from jax.sharding import PartitionSpec as P

PASSES = 2


def scale_parts(band_scale):
    hi = band_scale.astype(jnp.bfloat16)
    rest = band_scale - hi.astype(jnp.float32)
    mid = rest.astype(jnp.bfloat16)
    lo = (rest - mid.astype(jnp.float32)).astype(jnp.bfloat16)
    return jnp.concatenate([hi, mid, lo], axis=0)


def band_picks(band_values, parts):
    levels = parts.shape[0] // 3
    level_ids = jnp.arange(3 * levels, dtype=jnp.int32) % levels
    return (band_values[..., None] == level_ids).astype(jnp.bfloat16)


def first_kernel(live_tiles, x_ref, *refs):
    w_refs, (p_ref, s_ref, o_ref) = refs[:-3], refs[-3:]
    block = pl.program_id(0)
    step = pl.program_id(1)
    for k, w_ref in enumerate(w_refs):

        @pl.when((block == k) & (step < live_tiles[k]))
        def _():
            mixed = jnp.dot(x_ref[...], w_ref[...], preferred_element_type=jnp.float32)
            scale = jnp.dot(p_ref[...], s_ref[...], preferred_element_type=jnp.float32)
            v = mixed * scale
            o_ref[...] = (v * jax.nn.sigmoid(v)).astype(o_ref.dtype)


def last_live(step, live):
    return jnp.minimum(step, jnp.maximum(live - 1, 0))


ROW_TILE = 128


def first_hidden(rows, weights, picks, parts, live_tiles):
    n_blocks, n_rows, feat = rows.shape
    hid = weights[0].shape[1]
    n_pick = picks.shape[2]
    row_tile = min(n_rows, ROW_TILE)
    row_steps = n_rows // row_tile

    def weight_spec(k):
        return pl.BlockSpec((feat, hid), lambda s, i, j, live: (0, 0))

    def row_spec(width):
        return pl.BlockSpec(
            (None, row_tile, width), lambda s, i, j, live: (s, last_live(i, live[s]), 0)
        )

    return pl.pallas_call(
        first_kernel,
        grid_spec=pltpu.PrefetchScalarGridSpec(
            num_scalar_prefetch=1,
            grid=(n_blocks, row_steps, 1),
            in_specs=[row_spec(feat)]
            + [weight_spec(k) for k in range(n_blocks)]
            + [row_spec(n_pick), pl.BlockSpec((n_pick, hid), lambda s, i, j, live: (0, 0))],
            out_specs=pl.BlockSpec(
                (row_tile, hid), lambda s, i, j, live: (s * row_steps + last_live(i, live[s]), 0)
            ),
        ),
        out_shape=jax.ShapeDtypeStruct((n_blocks * n_rows, hid), jnp.bfloat16),
        cost_estimate=pl.CostEstimate(
            flops=2 * n_blocks * n_rows * hid * (feat + n_pick),
            transcendentals=n_blocks * n_rows * hid,
            bytes_accessed=2 * (n_blocks * n_rows * hid + n_blocks * feat * hid),
        ),
    )(live_tiles, rows, *weights, picks, parts)


def tail_kernel(live_tiles, h_ref, m_ref, w_ref, o_ref, *, row_steps):
    tile = pl.program_id(0)

    @pl.when(tile % row_steps < live_tiles[tile // row_steps])
    def _():
        middle = jnp.dot(h_ref[...], m_ref[...], preferred_element_type=jnp.float32)
        middle = (middle * jax.nn.sigmoid(middle)).astype(jnp.bfloat16)
        o_ref[...] = jnp.dot(middle, w_ref[...], preferred_element_type=jnp.float32)


def surrogate_tail(hidden, middle_weight, out_weight, live_tiles, n_blocks):
    n_all, hid = hidden.shape
    mid = middle_weight.shape[1]
    out_width = out_weight.shape[1]
    row_tile = min(n_all // n_blocks, ROW_TILE)
    row_steps = n_all // n_blocks // row_tile

    def tile_index(t, live):
        return (t // row_steps) * row_steps + last_live(t % row_steps, live[t // row_steps])

    return pl.pallas_call(
        functools.partial(tail_kernel, row_steps=row_steps),
        grid_spec=pltpu.PrefetchScalarGridSpec(
            num_scalar_prefetch=1,
            grid=(n_blocks * row_steps,),
            in_specs=[
                pl.BlockSpec((row_tile, hid), lambda t, live: (tile_index(t, live), 0)),
                pl.BlockSpec((hid, mid), lambda t, live: (0, 0)),
                pl.BlockSpec((mid, out_width), lambda t, live: (0, 0)),
            ],
            out_specs=pl.BlockSpec((row_tile, out_width), lambda t, live: (tile_index(t, live), 0)),
        ),
        out_shape=jax.ShapeDtypeStruct((n_all, out_width), jnp.float32),
        compiler_params=pltpu.CompilerParams(vmem_limit_bytes=48 * 1024 * 1024),
        cost_estimate=pl.CostEstimate(
            flops=2 * n_all * mid * (hid + out_width),
            transcendentals=n_all * mid,
            bytes_accessed=2 * (n_all * hid + hid * mid + mid * out_width) + 4 * n_all * out_width,
        ),
    )(live_tiles, hidden, middle_weight, out_weight)


def xor_pairs(n, k):
    return [(i, i ^ k) for i in range(n)]


def per_device(
    strain_rows,
    bands,
    damaged,
    owner,
    first_layers,
    middle_weight,
    out_weight,
    band_scale,
    back_weight,
):
    n_sec = lax.axis_size("sec")
    n_dev = lax.axis_size("dev")
    assert n_sec & (n_sec - 1) == 0
    count_all = n_sec * n_dev
    list_rows = damaged.shape[0]
    slot_count = max(2, 2 * list_rows // count_all)
    group_slots = n_sec * slot_count
    feat_width = strain_rows.shape[1]

    block_first = [first_layers] + [
        lax.ppermute(first_layers, "sec", xor_pairs(n_sec, k)) for k in range(1, n_sec)
    ]
    parts = scale_parts(band_scale)

    features = jnp.take(strain_rows, damaged, axis=0)
    band_local = jnp.take(bands, damaged)
    target_owner = owner[:, 0]
    matches = (target_owner[:, None] == jnp.arange(count_all, dtype=jnp.int32)[None, :]).astype(
        jnp.int32
    )
    slot_rank = jnp.sum((jnp.cumsum(matches, axis=0) - 1) * matches, axis=1)
    owner_sec = target_owner // n_dev
    owner_dev = target_owner % n_dev
    target = owner_dev * group_slots + owner_sec * slot_count + slot_rank
    dispatch = (
        jnp.arange(n_dev * group_slots, dtype=jnp.int32)[:, None] == target[None, :]
    ).astype(jnp.bfloat16)
    packed = jnp.concatenate(
        [features, (band_local + 1).astype(jnp.bfloat16)[:, None]], axis=1
    )
    grp = jnp.dot(dispatch, packed, preferred_element_type=jnp.float32).astype(jnp.bfloat16)
    grp = grp.reshape(n_dev, n_sec, slot_count, feat_width + 1)
    xor_table = np.bitwise_xor.outer(np.arange(n_sec), np.arange(n_sec)).reshape(-1)
    send = jnp.take(grp, jnp.asarray(xor_table, jnp.int32), axis=1)
    send = send.reshape(n_dev, n_sec, n_sec, slot_count, feat_width + 1).transpose(1, 0, 2, 3, 4)
    send = send.reshape(count_all, group_slots, feat_width + 1)
    got = lax.all_to_all(send, ("sec", "dev"), split_axis=0, concat_axis=0, tiled=True)
    got = got.reshape(count_all, n_sec, slot_count, feat_width + 1).transpose(1, 0, 2, 3)
    got = got.reshape(n_sec, count_all * slot_count, feat_width + 1)
    flag = got[:, :, feat_width].astype(jnp.int32)
    live = flag > 0
    n_rows = got.shape[1]
    live_count = jnp.sum(live.astype(jnp.int32), axis=1)
    place = jnp.where(
        live,
        jnp.cumsum(live.astype(jnp.int32), axis=1) - 1,
        live_count[:, None] + jnp.cumsum((~live).astype(jnp.int32), axis=1) - 1,
    )
    moves = (place[:, None, :] == jnp.arange(n_rows, dtype=jnp.int32)[None, :, None]).astype(
        jnp.bfloat16
    )
    got = jnp.einsum("kpr,krf->kpf", moves, got, preferred_element_type=jnp.float32).astype(
        jnp.bfloat16
    )
    row_tile = min(n_rows, ROW_TILE)
    live_tiles = (live_count + row_tile - 1) // row_tile
    rows = got[:, :, :feat_width]
    picks = band_picks(got[:, :, feat_width].astype(jnp.int32) - 1, parts)

    result = None
    for segment_index in range(PASSES):
        hidden = first_hidden(rows, block_first, picks, parts, live_tiles)
        partial = surrogate_tail(hidden, middle_weight, out_weight, live_tiles, n_sec).reshape(
            n_sec, rows.shape[1], -1
        )
        own_sum = partial[0]
        for k in range(1, n_sec):
            own_sum = own_sum + lax.ppermute(partial[k], "sec", xor_pairs(n_sec, k))
        own_values = own_sum.astype(jnp.bfloat16)
        if segment_index + 1 < PASSES:
            values = jnp.stack(
                [own_values]
                + [lax.ppermute(own_values, "sec", xor_pairs(n_sec, k)) for k in range(1, n_sec)]
            )
            rows = (
                rows.astype(jnp.float32)
                + jnp.einsum("sro,of->srf", values, back_weight, preferred_element_type=jnp.float32)
            ).astype(jnp.bfloat16)
        else:
            out_width = own_values.shape[1]
            own_values = jnp.take(own_values, place[0], axis=0)
            back = lax.all_to_all(
                own_values.reshape(count_all, slot_count, out_width),
                ("sec", "dev"),
                split_axis=0,
                concat_axis=0,
                tiled=True,
            )
            home = target_owner * slot_count + slot_rank
            result = jnp.take(back.reshape(count_all * slot_count, out_width), home, axis=0)
    return result


def solution(mesh):
    in_specs = (
        P(("sec", "dev"), None),
        P(("sec", "dev")),
        P(("sec", "dev")),
        P(("sec", "dev"), None),
        P(("sec", "dev"), None),
        P(None, "sec"),
        P("sec", None),
        P(),
        P(),
    )
    out_specs = P(("sec", "dev"), None)
    return jax.shard_map(
        per_device, mesh=mesh, in_specs=in_specs, out_specs=out_specs, check_vma=False
    )
```

```python
import jax
import jax.numpy as jnp
import numpy as np
from jax import lax
from jax.experimental import pallas as pl
from jax.experimental.pallas import tpu as pltpu
from jax.sharding import PartitionSpec as P

PASSES = 2


def scale_parts(band_scale):
    hi = band_scale.astype(jnp.bfloat16)
    rest = band_scale - hi.astype(jnp.float32)
    mid = rest.astype(jnp.bfloat16)
    lo = (rest - mid.astype(jnp.float32)).astype(jnp.bfloat16)
    return jnp.concatenate([hi, mid, lo], axis=0)


def band_picks(band_values, parts):
    levels = parts.shape[0] // 3
    level_ids = jnp.arange(3 * levels, dtype=jnp.int32) % levels
    return (band_values[..., None] == level_ids).astype(jnp.bfloat16)


CHUNK = 512


def pass_kernel(x_ref, *refs):
    w_refs, (p_ref, s_ref, m_ref, u_ref, o_ref) = refs[:-5], refs[-5:]
    block = pl.program_id(0)
    hid = s_ref.shape[1]
    for k, w_ref in enumerate(w_refs):

        @pl.when(block == k)
        def _():
            x = x_ref[...]
            p = p_ref[...]
            acc = None
            for c in range(hid // CHUNK):
                cols = slice(c * CHUNK, (c + 1) * CHUNK)
                mixed = jnp.dot(x, w_ref[:, cols], preferred_element_type=jnp.float32)
                scale = jnp.dot(p, s_ref[:, cols], preferred_element_type=jnp.float32)
                v = mixed * scale
                h = (v * jax.nn.sigmoid(v)).astype(jnp.bfloat16)
                part = jnp.dot(h, m_ref[cols, :], preferred_element_type=jnp.float32)
                acc = part if acc is None else acc + part
            middle = (acc * jax.nn.sigmoid(acc)).astype(jnp.bfloat16)
            o_ref[...] = jnp.dot(middle, u_ref[...], preferred_element_type=jnp.float32)


def pass_values(rows, weights, picks, parts, middle_weight, out_weight):
    n_blocks, n_rows, feat = rows.shape
    hid = weights[0].shape[1]
    mid = middle_weight.shape[1]
    out_width = out_weight.shape[1]
    n_pick = picks.shape[2]
    return pl.pallas_call(
        pass_kernel,
        grid=(n_blocks,),
        in_specs=[pl.BlockSpec((None, n_rows, feat), lambda s: (s, 0, 0))]
        + [pl.BlockSpec((feat, hid), lambda s: (0, 0)) for _ in range(n_blocks)]
        + [
            pl.BlockSpec((None, n_rows, n_pick), lambda s: (s, 0, 0)),
            pl.BlockSpec((n_pick, hid), lambda s: (0, 0)),
            pl.BlockSpec((hid, mid), lambda s: (0, 0)),
            pl.BlockSpec((mid, out_width), lambda s: (0, 0)),
        ],
        out_specs=pl.BlockSpec((n_rows, out_width), lambda s: (s, 0)),
        out_shape=jax.ShapeDtypeStruct((n_blocks * n_rows, out_width), jnp.float32),
        compiler_params=pltpu.CompilerParams(vmem_limit_bytes=60 * 1024 * 1024),
        cost_estimate=pl.CostEstimate(
            flops=2 * n_blocks * n_rows * (hid * (feat + n_pick + mid) + mid * out_width),
            transcendentals=n_blocks * n_rows * (hid + mid),
            bytes_accessed=2 * (n_blocks * feat * hid + hid * mid + mid * out_width)
            + 4 * n_blocks * n_rows * out_width,
        ),
    )(rows, *weights, picks, parts, middle_weight, out_weight)


def xor_pairs(n, k):
    return [(i, i ^ k) for i in range(n)]


def per_device(
    strain_rows,
    bands,
    damaged,
    owner,
    first_layers,
    middle_weight,
    out_weight,
    band_scale,
    back_weight,
):
    n_sec = lax.axis_size("sec")
    n_dev = lax.axis_size("dev")
    assert n_sec & (n_sec - 1) == 0
    count_all = n_sec * n_dev
    list_rows = damaged.shape[0]
    slot_count = max(2, 2 * list_rows // count_all)
    group_slots = n_sec * slot_count
    feat_width = strain_rows.shape[1]

    block_first = [first_layers] + [
        lax.ppermute(first_layers, "sec", xor_pairs(n_sec, k)) for k in range(1, n_sec)
    ]
    parts = scale_parts(band_scale)

    features = jnp.take(strain_rows, damaged, axis=0)
    band_local = jnp.take(bands, damaged)
    target_owner = owner[:, 0]
    matches = (target_owner[:, None] == jnp.arange(count_all, dtype=jnp.int32)[None, :]).astype(
        jnp.int32
    )
    slot_rank = jnp.sum((jnp.cumsum(matches, axis=0) - 1) * matches, axis=1)
    owner_sec = target_owner // n_dev
    owner_dev = target_owner % n_dev
    target = owner_dev * group_slots + owner_sec * slot_count + slot_rank
    dispatch = (
        jnp.arange(n_dev * group_slots, dtype=jnp.int32)[:, None] == target[None, :]
    ).astype(jnp.bfloat16)
    packed = jnp.concatenate(
        [features, band_local.astype(jnp.bfloat16)[:, None]], axis=1
    )
    grp = jnp.dot(dispatch, packed, preferred_element_type=jnp.float32).astype(jnp.bfloat16)
    grp = grp.reshape(n_dev, n_sec, slot_count, feat_width + 1)
    xor_table = np.bitwise_xor.outer(np.arange(n_sec), np.arange(n_sec)).reshape(-1)
    send = jnp.take(grp, jnp.asarray(xor_table, jnp.int32), axis=1)
    send = send.reshape(n_dev, n_sec, n_sec, slot_count, feat_width + 1).transpose(1, 0, 2, 3, 4)
    send = send.reshape(count_all, group_slots, feat_width + 1)
    got = lax.all_to_all(send, ("sec", "dev"), split_axis=0, concat_axis=0, tiled=True)
    got = got.reshape(count_all, n_sec, slot_count, feat_width + 1).transpose(1, 0, 2, 3)
    got = got.reshape(n_sec, count_all * slot_count, feat_width + 1)
    rows = got[:, :, :feat_width]
    picks = band_picks(got[:, :, feat_width].astype(jnp.int32), parts)

    result = None
    for segment_index in range(PASSES):
        partial = pass_values(rows, block_first, picks, parts, middle_weight, out_weight).reshape(
            n_sec, rows.shape[1], -1
        )
        own_sum = partial[0]
        for k in range(1, n_sec):
            own_sum = own_sum + lax.ppermute(partial[k], "sec", xor_pairs(n_sec, k))
        own_values = own_sum.astype(jnp.bfloat16)
        if segment_index + 1 < PASSES:
            values = jnp.stack(
                [own_values]
                + [lax.ppermute(own_values, "sec", xor_pairs(n_sec, k)) for k in range(1, n_sec)]
            )
            rows = (
                rows.astype(jnp.float32)
                + jnp.einsum("sro,of->srf", values, back_weight, preferred_element_type=jnp.float32)
            ).astype(jnp.bfloat16)
        else:
            out_width = own_values.shape[1]
            back = lax.all_to_all(
                own_values.reshape(count_all, slot_count, out_width),
                ("sec", "dev"),
                split_axis=0,
                concat_axis=0,
                tiled=True,
            )
            home = target_owner * slot_count + slot_rank
            result = jnp.take(back.reshape(count_all * slot_count, out_width), home, axis=0)
    return result


def solution(mesh):
    in_specs = (
        P(("sec", "dev"), None),
        P(("sec", "dev")),
        P(("sec", "dev")),
        P(("sec", "dev"), None),
        P(("sec", "dev"), None),
        P(None, "sec"),
        P("sec", None),
        P(),
        P(),
    )
    out_specs = P(("sec", "dev"), None)
    return jax.shard_map(
        per_device, mesh=mesh, in_specs=in_specs, out_specs=out_specs, check_vma=False
    )
```

```python
import jax
import jax.numpy as jnp
import numpy as np
from jax import lax
from jax.experimental import pallas as pl
from jax.experimental.pallas import tpu as pltpu
from jax.sharding import PartitionSpec as P

PASSES = 2


def scale_parts(band_scale):
    hi = band_scale.astype(jnp.bfloat16)
    rest = band_scale - hi.astype(jnp.float32)
    mid = rest.astype(jnp.bfloat16)
    lo = (rest - mid.astype(jnp.float32)).astype(jnp.bfloat16)
    return jnp.concatenate([hi, mid, lo], axis=0)


def band_picks(band_values, parts):
    levels = parts.shape[0] // 3
    level_ids = jnp.arange(3 * levels, dtype=jnp.int32) % levels
    return (band_values[..., None] == level_ids).astype(jnp.bfloat16)


CHUNK = 2048


def pass_kernel(x_ref, *refs):
    w_refs, (p_ref, s_ref, m_ref, u_ref, o_ref) = refs[:-5], refs[-5:]
    block = pl.program_id(0)
    hid = s_ref.shape[1]
    for k, w_ref in enumerate(w_refs):

        @pl.when(block == k)
        def _():
            x = x_ref[...]
            p = p_ref[...]
            acc = None
            for c in range(hid // CHUNK):
                cols = slice(c * CHUNK, (c + 1) * CHUNK)
                mixed = jnp.dot(x, w_ref[:, cols], preferred_element_type=jnp.float32)
                scale = jnp.dot(p, s_ref[:, cols], preferred_element_type=jnp.float32)
                v = mixed * scale
                h = (v * jax.nn.sigmoid(v)).astype(jnp.bfloat16)
                part = jnp.dot(h, m_ref[cols, :], preferred_element_type=jnp.float32)
                acc = part if acc is None else acc + part
            middle = (acc * jax.nn.sigmoid(acc)).astype(jnp.bfloat16)
            o_ref[...] = jnp.dot(middle, u_ref[...], preferred_element_type=jnp.float32)


def pass_values(rows, weights, picks, parts, middle_weight, out_weight):
    n_blocks, n_rows, feat = rows.shape
    hid = weights[0].shape[1]
    mid = middle_weight.shape[1]
    out_width = out_weight.shape[1]
    n_pick = picks.shape[2]
    return pl.pallas_call(
        pass_kernel,
        grid=(n_blocks,),
        in_specs=[pl.BlockSpec((None, n_rows, feat), lambda s: (s, 0, 0))]
        + [pl.BlockSpec((feat, hid), lambda s: (0, 0)) for _ in range(n_blocks)]
        + [
            pl.BlockSpec((None, n_rows, n_pick), lambda s: (s, 0, 0)),
            pl.BlockSpec((n_pick, hid), lambda s: (0, 0)),
            pl.BlockSpec((hid, mid), lambda s: (0, 0)),
            pl.BlockSpec((mid, out_width), lambda s: (0, 0)),
        ],
        out_specs=pl.BlockSpec((n_rows, out_width), lambda s: (s, 0)),
        out_shape=jax.ShapeDtypeStruct((n_blocks * n_rows, out_width), jnp.float32),
        compiler_params=pltpu.CompilerParams(vmem_limit_bytes=60 * 1024 * 1024),
        cost_estimate=pl.CostEstimate(
            flops=2 * n_blocks * n_rows * (hid * (feat + n_pick + mid) + mid * out_width),
            transcendentals=n_blocks * n_rows * (hid + mid),
            bytes_accessed=2 * (n_blocks * feat * hid + hid * mid + mid * out_width)
            + 4 * n_blocks * n_rows * out_width,
        ),
    )(rows, *weights, picks, parts, middle_weight, out_weight)


def xor_pairs(n, k):
    return [(i, i ^ k) for i in range(n)]


def per_device(
    strain_rows,
    bands,
    damaged,
    owner,
    first_layers,
    middle_weight,
    out_weight,
    band_scale,
    back_weight,
):
    n_sec = lax.axis_size("sec")
    n_dev = lax.axis_size("dev")
    assert n_sec & (n_sec - 1) == 0
    count_all = n_sec * n_dev
    list_rows = damaged.shape[0]
    slot_count = max(2, 2 * list_rows // count_all)
    group_slots = n_sec * slot_count
    feat_width = strain_rows.shape[1]

    block_first = [first_layers] + [
        lax.ppermute(first_layers, "sec", xor_pairs(n_sec, k)) for k in range(1, n_sec)
    ]
    parts = scale_parts(band_scale)

    features = jnp.take(strain_rows, damaged, axis=0)
    band_local = jnp.take(bands, damaged)
    target_owner = owner[:, 0]
    matches = (target_owner[:, None] == jnp.arange(count_all, dtype=jnp.int32)[None, :]).astype(
        jnp.int32
    )
    slot_rank = jnp.sum((jnp.cumsum(matches, axis=0) - 1) * matches, axis=1)
    owner_sec = target_owner // n_dev
    owner_dev = target_owner % n_dev
    target = owner_dev * group_slots + owner_sec * slot_count + slot_rank
    dispatch = (
        jnp.arange(n_dev * group_slots, dtype=jnp.int32)[:, None] == target[None, :]
    ).astype(jnp.bfloat16)
    packed = jnp.concatenate(
        [features, band_local.astype(jnp.bfloat16)[:, None]], axis=1
    )
    grp = jnp.dot(dispatch, packed, preferred_element_type=jnp.float32).astype(jnp.bfloat16)
    grp = grp.reshape(n_dev, n_sec, slot_count, feat_width + 1)
    xor_table = np.bitwise_xor.outer(np.arange(n_sec), np.arange(n_sec)).reshape(-1)
    send = jnp.take(grp, jnp.asarray(xor_table, jnp.int32), axis=1)
    send = send.reshape(n_dev, n_sec, n_sec, slot_count, feat_width + 1).transpose(1, 0, 2, 3, 4)
    send = send.reshape(count_all, group_slots, feat_width + 1)
    got = lax.all_to_all(send, ("sec", "dev"), split_axis=0, concat_axis=0, tiled=True)
    got = got.reshape(count_all, n_sec, slot_count, feat_width + 1).transpose(1, 0, 2, 3)
    got = got.reshape(n_sec, count_all * slot_count, feat_width + 1)
    rows = got[:, :, :feat_width]
    picks = band_picks(got[:, :, feat_width].astype(jnp.int32), parts)

    result = None
    for segment_index in range(PASSES):
        partial = pass_values(rows, block_first, picks, parts, middle_weight, out_weight).reshape(
            n_sec, rows.shape[1], -1
        )
        own_sum = partial[0]
        for k in range(1, n_sec):
            own_sum = own_sum + lax.ppermute(partial[k], "sec", xor_pairs(n_sec, k))
        own_values = own_sum.astype(jnp.bfloat16)
        if segment_index + 1 < PASSES:
            values = jnp.stack(
                [own_values]
                + [lax.ppermute(own_values, "sec", xor_pairs(n_sec, k)) for k in range(1, n_sec)]
            )
            rows = (
                rows.astype(jnp.float32)
                + jnp.einsum("sro,of->srf", values, back_weight, preferred_element_type=jnp.float32)
            ).astype(jnp.bfloat16)
        else:
            out_width = own_values.shape[1]
            back = lax.all_to_all(
                own_values.reshape(count_all, slot_count, out_width),
                ("sec", "dev"),
                split_axis=0,
                concat_axis=0,
                tiled=True,
            )
            home = target_owner * slot_count + slot_rank
            result = jnp.take(back.reshape(count_all * slot_count, out_width), home, axis=0)
    return result


def solution(mesh):
    in_specs = (
        P(("sec", "dev"), None),
        P(("sec", "dev")),
        P(("sec", "dev")),
        P(("sec", "dev"), None),
        P(("sec", "dev"), None),
        P(None, "sec"),
        P("sec", None),
        P(),
        P(),
    )
    out_specs = P(("sec", "dev"), None)
    return jax.shard_map(
        per_device, mesh=mesh, in_specs=in_specs, out_specs=out_specs, check_vma=False
    )
```

```python
import jax
import jax.numpy as jnp
import numpy as np
from jax import lax
from jax.experimental import pallas as pl
from jax.experimental.pallas import tpu as pltpu
from jax.sharding import PartitionSpec as P

PASSES = 2


def scale_parts(band_scale):
    hi = band_scale.astype(jnp.bfloat16)
    rest = band_scale - hi.astype(jnp.float32)
    mid = rest.astype(jnp.bfloat16)
    lo = (rest - mid.astype(jnp.float32)).astype(jnp.bfloat16)
    return jnp.concatenate([hi, mid, lo], axis=0)


def band_picks(band_values, parts):
    levels = parts.shape[0] // 3
    level_ids = jnp.arange(3 * levels, dtype=jnp.int32) % levels
    return (band_values[..., None] == level_ids).astype(jnp.bfloat16)


CHUNK = 2048


def pass_kernel(x_ref, *refs):
    w_refs, (p_ref, s_ref, m_ref, u_ref, o_ref) = refs[:-5], refs[-5:]
    block = pl.program_id(0)
    hid = s_ref.shape[1]
    for k, w_ref in enumerate(w_refs):

        @pl.when(block == k)
        def _():
            x = x_ref[...]
            p = p_ref[...]
            acc = None
            for c in range(hid // CHUNK):
                cols = slice(c * CHUNK, (c + 1) * CHUNK)
                mixed = jnp.dot(x, w_ref[:, cols], preferred_element_type=jnp.float32)
                scale = jnp.dot(p, s_ref[:, cols], preferred_element_type=jnp.float32)
                v = mixed * scale
                h = (v * jax.nn.sigmoid(v)).astype(jnp.bfloat16)
                part = jnp.dot(h, m_ref[cols, :], preferred_element_type=jnp.float32)
                acc = part if acc is None else acc + part
            middle = (acc * jax.nn.sigmoid(acc)).astype(jnp.bfloat16)
            o_ref[...] = jnp.dot(middle, u_ref[...], preferred_element_type=jnp.float32)


def pass_values(rows, weights, picks, parts, middle_weight, out_weight):
    n_blocks, n_rows, feat = rows.shape
    hid = weights[0].shape[1]
    mid = middle_weight.shape[1]
    out_width = out_weight.shape[1]
    n_pick = picks.shape[2]
    return pl.pallas_call(
        pass_kernel,
        grid=(n_blocks,),
        in_specs=[pl.BlockSpec((None, n_rows, feat), lambda s: (s, 0, 0))]
        + [pl.BlockSpec((feat, hid), lambda s: (0, 0)) for _ in range(n_blocks)]
        + [
            pl.BlockSpec((None, n_rows, n_pick), lambda s: (s, 0, 0)),
            pl.BlockSpec((n_pick, hid), lambda s: (0, 0)),
            pl.BlockSpec((hid, mid), lambda s: (0, 0)),
            pl.BlockSpec((mid, out_width), lambda s: (0, 0)),
        ],
        out_specs=pl.BlockSpec((n_rows, out_width), lambda s: (s, 0)),
        out_shape=jax.ShapeDtypeStruct((n_blocks * n_rows, out_width), jnp.float32),
        compiler_params=pltpu.CompilerParams(vmem_limit_bytes=60 * 1024 * 1024),
        cost_estimate=pl.CostEstimate(
            flops=2 * n_blocks * n_rows * (hid * (feat + n_pick + mid) + mid * out_width),
            transcendentals=n_blocks * n_rows * (hid + mid),
            bytes_accessed=2 * (n_blocks * feat * hid + hid * mid + mid * out_width)
            + 4 * n_blocks * n_rows * out_width,
        ),
    )(rows, *weights, picks, parts, middle_weight, out_weight)


def xor_pairs(n, k):
    return [(i, i ^ k) for i in range(n)]


def per_device(
    strain_rows,
    bands,
    damaged,
    owner,
    first_layers,
    middle_weight,
    out_weight,
    band_scale,
    back_weight,
):
    n_sec = lax.axis_size("sec")
    n_dev = lax.axis_size("dev")
    assert n_sec & (n_sec - 1) == 0
    count_all = n_sec * n_dev
    list_rows = damaged.shape[0]
    slot_count = max(2, 2 * list_rows // count_all)
    group_slots = n_sec * slot_count
    feat_width = strain_rows.shape[1]

    block_first = [first_layers] + [
        lax.ppermute(first_layers, "sec", xor_pairs(n_sec, k)) for k in range(1, n_sec)
    ]
    parts = scale_parts(band_scale)

    features = jnp.take(strain_rows, damaged, axis=0)
    band_local = jnp.take(bands, damaged)
    target_owner = owner[:, 0]
    matches = (target_owner[:, None] == jnp.arange(count_all, dtype=jnp.int32)[None, :]).astype(
        jnp.int32
    )
    slot_rank = jnp.sum((jnp.cumsum(matches, axis=0) - 1) * matches, axis=1)
    owner_sec = target_owner // n_dev
    owner_dev = target_owner % n_dev
    target = owner_dev * group_slots + owner_sec * slot_count + slot_rank
    dispatch = (
        jnp.arange(n_dev * group_slots, dtype=jnp.int32)[:, None] == target[None, :]
    ).astype(jnp.bfloat16)
    packed = jnp.concatenate(
        [features, band_local.astype(jnp.bfloat16)[:, None]], axis=1
    )
    grp = jnp.dot(dispatch, packed, preferred_element_type=jnp.float32).astype(jnp.bfloat16)
    grp = grp.reshape(n_dev, n_sec, slot_count, feat_width + 1)
    xor_table = np.bitwise_xor.outer(np.arange(n_sec), np.arange(n_sec)).reshape(-1)
    send = jnp.take(grp, jnp.asarray(xor_table, jnp.int32), axis=1)
    send = send.reshape(n_dev, n_sec, n_sec, slot_count, feat_width + 1).transpose(1, 0, 2, 3, 4)
    send = send.reshape(count_all, group_slots, feat_width + 1)
    got = lax.all_to_all(send, ("sec", "dev"), split_axis=0, concat_axis=0, tiled=True)
    got = got.reshape(count_all, n_sec, slot_count, feat_width + 1).transpose(1, 0, 2, 3)
    got = got.reshape(n_sec, count_all * slot_count, feat_width + 1)
    sec_turn = jnp.bitwise_xor(jnp.arange(n_sec, dtype=jnp.int32), lax.axis_index("sec"))
    rows = got[:, :, :feat_width]
    picks = band_picks(got[:, :, feat_width].astype(jnp.int32), parts)

    result = None
    for segment_index in range(PASSES):
        partial = pass_values(rows, block_first, picks, parts, middle_weight, out_weight).reshape(
            n_sec, rows.shape[1], -1
        )
        by_owner = jnp.take(partial, sec_turn, axis=0)
        own_sum = jnp.sum(
            lax.all_to_all(by_owner, "sec", split_axis=0, concat_axis=0, tiled=True), axis=0
        )
        own_values = own_sum.astype(jnp.bfloat16)
        if segment_index + 1 < PASSES:
            spread = jnp.broadcast_to(own_values[None], (n_sec,) + own_values.shape)
            values = jnp.take(
                lax.all_to_all(spread, "sec", split_axis=0, concat_axis=0, tiled=True),
                sec_turn,
                axis=0,
            )
            rows = (
                rows.astype(jnp.float32)
                + jnp.einsum("sro,of->srf", values, back_weight, preferred_element_type=jnp.float32)
            ).astype(jnp.bfloat16)
        else:
            out_width = own_values.shape[1]
            back = lax.all_to_all(
                own_values.reshape(count_all, slot_count, out_width),
                ("sec", "dev"),
                split_axis=0,
                concat_axis=0,
                tiled=True,
            )
            home = target_owner * slot_count + slot_rank
            result = jnp.take(back.reshape(count_all * slot_count, out_width), home, axis=0)
    return result


def solution(mesh):
    in_specs = (
        P(("sec", "dev"), None),
        P(("sec", "dev")),
        P(("sec", "dev")),
        P(("sec", "dev"), None),
        P(("sec", "dev"), None),
        P(None, "sec"),
        P("sec", None),
        P(),
        P(),
    )
    out_specs = P(("sec", "dev"), None)
    return jax.shard_map(
        per_device, mesh=mesh, in_specs=in_specs, out_specs=out_specs, check_vma=False
    )
```

```python
import jax
import jax.numpy as jnp
import numpy as np
from jax import lax
from jax.experimental import pallas as pl
from jax.experimental.pallas import tpu as pltpu
from jax.sharding import PartitionSpec as P

PASSES = 2


def scale_parts(band_scale):
    hi = band_scale.astype(jnp.bfloat16)
    rest = band_scale - hi.astype(jnp.float32)
    mid = rest.astype(jnp.bfloat16)
    lo = (rest - mid.astype(jnp.float32)).astype(jnp.bfloat16)
    return jnp.concatenate([hi, mid, lo], axis=0)


def band_picks(band_values, parts):
    levels = parts.shape[0] // 3
    level_ids = jnp.arange(3 * levels, dtype=jnp.int32) % levels
    return (band_values[..., None] == level_ids).astype(jnp.bfloat16)


CHUNK = 2048


def pass_kernel(x_ref, *refs):
    w_refs, (p_ref, s_ref, m_ref, u_ref, o_ref) = refs[:-5], refs[-5:]
    block = pl.program_id(0)
    hid = s_ref.shape[1]
    for k, w_ref in enumerate(w_refs):

        @pl.when(block == k)
        def _():
            x = x_ref[...]
            p = p_ref[...]
            acc = None
            for c in range(hid // CHUNK):
                cols = slice(c * CHUNK, (c + 1) * CHUNK)
                mixed = jnp.dot(x, w_ref[:, cols], preferred_element_type=jnp.float32)
                scale = jnp.dot(p, s_ref[:, cols], preferred_element_type=jnp.float32)
                v = mixed * scale
                h = (v * jax.nn.sigmoid(v)).astype(jnp.bfloat16)
                part = jnp.dot(h, m_ref[cols, :], preferred_element_type=jnp.float32)
                acc = part if acc is None else acc + part
            middle = (acc * jax.nn.sigmoid(acc)).astype(jnp.bfloat16)
            o_ref[...] = jnp.dot(middle, u_ref[...], preferred_element_type=jnp.float32)


def pass_values(rows, weights, picks, parts, middle_weight, out_weight):
    n_blocks, n_rows, feat = rows.shape
    hid = weights[0].shape[1]
    mid = middle_weight.shape[1]
    out_width = out_weight.shape[1]
    n_pick = picks.shape[2]
    return pl.pallas_call(
        pass_kernel,
        grid=(n_blocks,),
        in_specs=[pl.BlockSpec((None, n_rows, feat), lambda s: (s, 0, 0))]
        + [pl.BlockSpec((feat, hid), lambda s: (0, 0)) for _ in range(n_blocks)]
        + [
            pl.BlockSpec((None, n_rows, n_pick), lambda s: (s, 0, 0)),
            pl.BlockSpec((n_pick, hid), lambda s: (0, 0)),
            pl.BlockSpec((hid, mid), lambda s: (0, 0)),
            pl.BlockSpec((mid, out_width), lambda s: (0, 0)),
        ],
        out_specs=pl.BlockSpec((n_rows, out_width), lambda s: (s, 0)),
        out_shape=jax.ShapeDtypeStruct((n_blocks * n_rows, out_width), jnp.float32),
        compiler_params=pltpu.CompilerParams(vmem_limit_bytes=60 * 1024 * 1024),
        cost_estimate=pl.CostEstimate(
            flops=2 * n_blocks * n_rows * (hid * (feat + n_pick + mid) + mid * out_width),
            transcendentals=n_blocks * n_rows * (hid + mid),
            bytes_accessed=2 * (n_blocks * feat * hid + hid * mid + mid * out_width)
            + 4 * n_blocks * n_rows * out_width,
        ),
    )(rows, *weights, picks, parts, middle_weight, out_weight)


def xor_pairs(n, k):
    return [(i, i ^ k) for i in range(n)]


def per_device(
    strain_rows,
    bands,
    damaged,
    owner,
    first_layers,
    middle_weight,
    out_weight,
    band_scale,
    back_weight,
):
    n_sec = lax.axis_size("sec")
    n_dev = lax.axis_size("dev")
    assert n_sec & (n_sec - 1) == 0
    count_all = n_sec * n_dev
    list_rows = damaged.shape[0]
    slot_count = max(2, 2 * list_rows // count_all)
    group_slots = n_sec * slot_count
    feat_width = strain_rows.shape[1]

    block_first = [first_layers] + [
        lax.ppermute(first_layers, "sec", xor_pairs(n_sec, k)) for k in range(1, n_sec)
    ]
    parts = scale_parts(band_scale)

    features = jnp.take(strain_rows, damaged, axis=0)
    band_local = jnp.take(bands, damaged)
    target_owner = owner[:, 0]
    matches = (target_owner[:, None] == jnp.arange(count_all, dtype=jnp.int32)[None, :]).astype(
        jnp.int32
    )
    slot_rank = jnp.sum((jnp.cumsum(matches, axis=0) - 1) * matches, axis=1)
    owner_sec = target_owner // n_dev
    owner_dev = target_owner % n_dev
    target = owner_dev * group_slots + owner_sec * slot_count + slot_rank
    dispatch = (
        jnp.arange(n_dev * group_slots, dtype=jnp.int32)[:, None] == target[None, :]
    ).astype(jnp.bfloat16)
    packed = jnp.concatenate(
        [features, band_local.astype(jnp.bfloat16)[:, None]], axis=1
    )
    grp = jnp.dot(dispatch, packed, preferred_element_type=jnp.float32).astype(jnp.bfloat16)
    grp = grp.reshape(n_dev, n_sec, slot_count, feat_width + 1)
    xor_table = np.bitwise_xor.outer(np.arange(n_sec), np.arange(n_sec)).reshape(-1)
    send = jnp.take(grp, jnp.asarray(xor_table, jnp.int32), axis=1)
    send = send.reshape(n_dev, n_sec, n_sec, slot_count, feat_width + 1).transpose(1, 0, 2, 3, 4)
    send = send.reshape(count_all, group_slots * (feat_width + 1))
    got = lax.all_to_all(send, ("sec", "dev"), split_axis=0, concat_axis=0, tiled=True)
    got = got.reshape(count_all, n_sec, slot_count, feat_width + 1).transpose(1, 0, 2, 3)
    got = got.reshape(n_sec, count_all * slot_count, feat_width + 1)
    rows = got[:, :, :feat_width]
    picks = band_picks(got[:, :, feat_width].astype(jnp.int32), parts)

    result = None
    for segment_index in range(PASSES):
        partial = pass_values(rows, block_first, picks, parts, middle_weight, out_weight).reshape(
            n_sec, rows.shape[1], -1
        )
        own_sum = partial[0]
        for k in range(1, n_sec):
            own_sum = own_sum + lax.ppermute(partial[k], "sec", xor_pairs(n_sec, k))
        own_values = own_sum.astype(jnp.bfloat16)
        if segment_index + 1 < PASSES:
            values = jnp.stack(
                [own_values]
                + [lax.ppermute(own_values, "sec", xor_pairs(n_sec, k)) for k in range(1, n_sec)]
            )
            rows = (
                rows.astype(jnp.float32)
                + jnp.einsum("sro,of->srf", values, back_weight, preferred_element_type=jnp.float32)
            ).astype(jnp.bfloat16)
        else:
            out_width = own_values.shape[1]
            back = lax.all_to_all(
                own_values.reshape(count_all, slot_count, out_width),
                ("sec", "dev"),
                split_axis=0,
                concat_axis=0,
                tiled=True,
            )
            home = target_owner * slot_count + slot_rank
            result = jnp.take(back.reshape(count_all * slot_count, out_width), home, axis=0)
    return result


def solution(mesh):
    in_specs = (
        P(("sec", "dev"), None),
        P(("sec", "dev")),
        P(("sec", "dev")),
        P(("sec", "dev"), None),
        P(("sec", "dev"), None),
        P(None, "sec"),
        P("sec", None),
        P(),
        P(),
    )
    out_specs = P(("sec", "dev"), None)
    return jax.shard_map(
        per_device, mesh=mesh, in_specs=in_specs, out_specs=out_specs, check_vma=False
    )
```
